256 devices in a mesh: dp: 16 (over x, y_lo, core), expert: 16 (over z, y_hi).
Axes of the slice: x: 4, y: 4 (y_hi: 2, y_lo: 2; y = y_hi * 2 + y_lo), z: 8, core: 2. Of those that a mesh axis runs over, the one named last changes fastest.
Arguments:
- tokens: bfloat16 [32768, 2048], P(('dp', 'expert')), may hold values from -6 to 6
- gain: float32 [2048], replicated, may hold values from 0.1 to 1.9
- expert_ids: int32 [32768, 8], P(('dp', 'expert')), may hold values from 0 to 15, all different within a row; in each aligned block of 128 rows (0 to 127, 128 to 255, ...) at most 96 rows name the same one
- gate_values: float32 [32768, 8], P(('dp', 'expert')), may hold values from 0.02 to 0.25
- w_gate: bfloat16 [16, 2048, 768], P('expert'), may hold values from -0.125 to 0.125
- w_up: bfloat16 [16, 2048, 768], P('expert'), may hold values from -0.125 to 0.125
- w_down: bfloat16 [16, 768, 2048], P('expert'), may hold values from -0.21875 to 0.21875
Outputs:
- mixed: bfloat16 [32768, 2048], P(('dp', 'expert'))
The draws below stay inside these ranges and needn't reach their ends.
Inputs may be any that keep to these rules, and one draw needn't show every extreme that they name: `expert_ids`: each row names 8 different experts. In the rows of one device no expert is named by more than 96 rows, and in every draw some expert is named by exactly 96 rows of some device.
All inputs are finite; a program needn't handle non-finite values.
Results may differ from the reference program's by a relative error of at most 0.018.
Values may be sent and summed in bfloat16 or wider, within the bound.
No kernel may reach another device: no remote copies, remote signals or barrier semaphores. Data moves between devices by JAX's collectives and lax.ppermute only.
A program may use at most 128 MiB of HBM per device.

```python
import math
import jax
import jax.numpy as jnp
import numpy as np
from jax import lax

D = 2048
FF = 768
TOK_DEV = 128
EXPERTS = 16
TOP = 8
CAP = 96
TOKENS = 32768


def block_scale(own_key, extent, shards, least, largest):
    level = 1.0
    for dim, blocks in shards:
        draws = jax.random.uniform(jax.random.fold_in(jax.random.fold_in(own_key, 6), dim), (blocks,), jnp.float32, least / len(shards), largest / len(shards))
        level = level * jnp.repeat(jnp.exp(draws), extent[dim] // blocks).reshape((-1,) + (1,) * (len(extent) - 1 - dim))
    return level


def shared_out(own_key, own, number, rows, amount, top, reach, slope):
    ranking = jax.random.permutation(own_key, amount)
    packed, common = portions_of(amount, rows * top, reach, slope, True), portions_of(amount, rows * top, reach, slope, False)
    places = jnp.arange(amount)

    def named(tallies, rotation):
        used = int((tallies > 0).sum())
        fixed = max(1, used // 4)
        shifted = fixed + (places - fixed + rotation * (used - fixed)) % max(1, amount - fixed)
        return jnp.zeros((amount,), jnp.int32).at[ranking[jnp.where(places < fixed, places, shifted)]].set(jnp.asarray(tallies, jnp.int32))

    tallies = jnp.where(number % 4 == 0, named(packed, number // 4), named(common, number - number // 4 - 1))
    mixed = jax.random.permutation(jax.random.fold_in(own, 3), amount)
    donor, sink = mixed[0:amount // 2 * 2:2], mixed[1:amount // 2 * 2:2]
    slack = jnp.minimum(tallies[donor] - 1, reach - tallies[sink]) // 2
    slack = jnp.where((donor == ranking[0]) | (sink == ranking[0]) | (tallies[sink] == 0), 0, jnp.maximum(slack, 0))
    shifted = jax.random.randint(jax.random.fold_in(own, 4), (amount // 2,), 0, 1 << 20) % (slack + 1)
    tallies = tallies.at[donor].add(-shifted).at[sink].add(shifted)
    items = jnp.searchsorted(jnp.cumsum(tallies), jnp.arange(rows * top), side="right").astype(jnp.int32)
    grid = items.reshape(top, rows).T
    grid = grid[jax.random.permutation(jax.random.fold_in(own, 1), rows)]
    rotation = jax.random.randint(jax.random.fold_in(own, 2), (rows, 1), 0, top)
    return jnp.take_along_axis(grid, (jnp.arange(top)[None, :] + rotation) % top, axis=1)


def portions_of(count, total, bound, lean, full):
    weights = [(1 << 20) // math.isqrt(grade ** lean) + 1 for grade in range(1, count + 1)]
    largest = bound if full else min(bound, max(-(-total // count), total * weights[0] // sum(weights)))
    least = 1 if total - largest >= count - 1 else 0
    holding, rest = [largest] + [least] * (count - 1), total - largest - least * (count - 1)
    while rest > 0:
        free = [i for i in range(1, count) if holding[i] < largest] or [i for i in range(1, count) if holding[i] < bound]
        pool, left = sum([weights[i] for i in free]), rest
        for i in free:
            addition = min(bound - holding[i], max(1, left * weights[i] // pool), rest)
            holding[i] = holding[i] + addition
            rest = rest - addition
    return np.array(holding)


def bell_draw(rng, extent, deviation, most, shards=(), kind=jnp.bfloat16):
    drawn = deviation * jax.random.normal(rng, extent, jnp.float32)
    if shards:
        drawn = drawn * block_scale(rng, extent, shards, -0.22, 0.18)
    return jnp.clip(drawn, -most, most).astype(kind)


def setup_inputs(seed: int = 0) -> dict:
    key_list = jax.random.split(jax.random.key(seed), 8)
    tokens = bell_draw(key_list[0], (TOKENS, D), 1.0, 6.0, ((0, 256),))
    gain = jnp.clip(1.0 + 0.18 * jax.random.normal(key_list[1], (D,), jnp.float32), 0.1, 1.9)
    expert_ids_keys = jax.random.split(jax.random.fold_in(key_list[2], 1), TOKENS // TOK_DEV)
    expert_ids_turns = jax.random.permutation(jax.random.fold_in(key_list[2], 3), TOKENS // TOK_DEV)
    expert_ids = jax.vmap(lambda own, number: shared_out(jax.random.fold_in(key_list[2], 2), own, number, TOK_DEV, EXPERTS, TOP, CAP, 2))(expert_ids_keys, expert_ids_turns).reshape((TOKENS, TOP))
    gate_values = jnp.clip(0.02 + 0.23 * jax.random.uniform(key_list[3], (TOKENS, TOP), jnp.float32) ** block_scale(key_list[3], (TOKENS, TOP), ((0, 256),), -0.2, 0.2), 0.02, 0.25)
    w_gate = bell_draw(key_list[4], (EXPERTS, D, FF), D ** -0.5, 0.125, ((0, 16),))
    w_up = bell_draw(key_list[5], (EXPERTS, D, FF), D ** -0.5, 0.125, ((0, 16),))
    w_down = bell_draw(key_list[6], (EXPERTS, FF, D), FF ** -0.5, 0.21875, ((0, 16),))
    return dict(tokens=tokens, gain=gain, expert_ids=expert_ids, gate_values=gate_values, w_gate=w_gate, w_up=w_up, w_down=w_down)


eps_value = 1e-06

def normalize(tokens, gain):
    values = tokens.astype(jnp.float32)
    meansq = lax.optimization_barrier(jnp.mean(values * values, axis=-1, keepdims=True))
    return (values * lax.rsqrt(meansq + eps_value) * gain.astype(jnp.float32)).astype(jnp.bfloat16)

def gate_dense(expert_ids, gate_values, number):
    labels = jnp.arange(number, dtype=jnp.int32)
    hits = (expert_ids[..., None] == labels).astype(jnp.float32)
    return lax.optimization_barrier(jnp.sum(hits * gate_values[..., None], axis=-2))

def dispatch_table(column, capacity):
    matched = (column > 0).astype(jnp.float32)
    slots = jnp.cumsum(matched, axis=-1) - 1.0
    places = jnp.arange(capacity).astype(jnp.float32)
    chosen = (slots[..., None, :] == places[:, None]) & (matched[..., None, :] > 0)
    return chosen.astype(jnp.bfloat16)

def expert_mlp(slot_rows, gate_matrix, up_matrix, down_matrix):
    gated = jnp.dot(slot_rows, gate_matrix, preferred_element_type=jnp.float32)
    upward = jnp.dot(slot_rows, up_matrix, preferred_element_type=jnp.float32)
    hidden = (jax.nn.silu(gated) * upward).astype(jnp.bfloat16)
    return jnp.dot(hidden, down_matrix, preferred_element_type=jnp.float32).astype(jnp.bfloat16)

def reference(tokens, gain, expert_ids, gate_values, w_gate, w_up, w_down):
    normed = normalize(tokens, gain)
    dense = gate_dense(expert_ids, gate_values, EXPERTS)
    blocks = TOKENS // TOK_DEV
    normed_blocks = normed.reshape(blocks, TOK_DEV, D).astype(jnp.float32)
    dense_blocks = dense.reshape(blocks, TOK_DEV, EXPERTS)

    def per_expert(total, index):
        column = jnp.take(dense_blocks, index, axis=2)
        table = dispatch_table(column, CAP).astype(jnp.float32)
        slot_rows = jnp.einsum('bct,btd->bcd', table, normed_blocks).astype(jnp.bfloat16)
        outputs = expert_mlp(slot_rows.reshape(blocks * CAP, D), w_gate[index], w_up[index], w_down[index])
        outputs = outputs.reshape(blocks, CAP, D).astype(jnp.float32)
        back = jnp.einsum('bct,bcd->btd', table, outputs)
        return (total + back * column[:, :, None], None)
    start_total = jnp.zeros((blocks, TOK_DEV, D), jnp.float32)
    total, unused = lax.scan(per_expert, start_total, jnp.arange(EXPERTS, dtype=jnp.int32))
    return total.reshape(TOKENS, D).astype(jnp.bfloat16)
```

```python
import jax
import jax.numpy as jnp
from jax import lax
from jax.sharding import PartitionSpec as P

eps_value = 1e-06


def normalize(tokens, gain):
    values = tokens.astype(jnp.float32)
    meansq = jnp.mean(values * values, axis=-1, keepdims=True)
    return (values * lax.rsqrt(meansq + eps_value) * gain).astype(jnp.bfloat16)


def gate_dense(expert_ids, gate_values, number):
    labels = jnp.arange(number, dtype=jnp.int32)
    hits = (expert_ids[..., None] == labels).astype(jnp.float32)
    return jnp.sum(hits * gate_values[..., None], axis=-2)


def dispatch_table(column, capacity):
    matched = (column > 0).astype(jnp.float32)
    slots = jnp.cumsum(matched, axis=-1) - 1.0
    places = jnp.arange(capacity).astype(jnp.float32)
    chosen = (slots[..., None, :] == places[:, None]) & (matched[..., None, :] > 0)
    return chosen


def expert_mlp(slot_rows, gate_matrix, up_matrix, down_matrix):
    gated = jnp.dot(slot_rows, gate_matrix, preferred_element_type=jnp.float32)
    upward = jnp.dot(slot_rows, up_matrix, preferred_element_type=jnp.float32)
    hidden = (jax.nn.silu(gated) * upward).astype(jnp.bfloat16)
    return jnp.dot(hidden, down_matrix, preferred_element_type=jnp.float32).astype(jnp.bfloat16)


def bf16_parts(values, count):
    parts = []
    rest = values
    for _ in range(count):
        head = lax.reduce_precision(rest, exponent_bits=8, mantissa_bits=7)
        parts.append(head.astype(jnp.bfloat16))
        rest = rest - head
    return parts


def local(tokens, gain, expert_ids, gate_values, w_gate, w_up, w_down):
    group = lax.axis_size("expert")
    local_rows, width = tokens.shape
    chosen_count = expert_ids.shape[1]
    number = group * w_gate.shape[0]
    capacity = local_rows * chosen_count // number * 3 // 2
    normed = normalize(tokens, gain)
    dense = gate_dense(expert_ids, gate_values, number)
    column = dense.T
    chosen = dispatch_table(column, capacity)
    table = chosen.astype(jnp.bfloat16)
    send = jnp.einsum("est,td->esd", table, normed, preferred_element_type=jnp.float32)
    send = send.astype(jnp.bfloat16)
    recv = lax.all_to_all(send, "expert", 0, 0, tiled=True)
    outputs = expert_mlp(recv.reshape(-1, width), w_gate[0], w_up[0], w_down[0])
    back = lax.all_to_all(outputs.reshape(group, -1, width), "expert", 0, 0, tiled=True)
    weights = jnp.where(chosen, column[:, None, :], 0.0)
    weights = weights.reshape(-1, local_rows)
    flat = back.reshape(-1, width)
    mixed = None
    for part in bf16_parts(weights, 3):
        term = lax.dot_general(
            part, flat, (((0,), (0,)), ((), ())), preferred_element_type=jnp.float32
        )
        mixed = term if mixed is None else mixed + term
    return mixed.astype(jnp.bfloat16)


def solution(mesh):
    return jax.shard_map(
        local,
        mesh=mesh,
        in_specs=(
            P(("dp", "expert"), None),
            P(),
            P(("dp", "expert"), None),
            P(("dp", "expert"), None),
            P("expert", None, None),
            P("expert", None, None),
            P("expert", None, None),
        ),
        out_specs=P(("dp", "expert"), None),
        check_vma=False,
    )
```

```python
import jax
import jax.numpy as jnp
from jax import lax
from jax.sharding import PartitionSpec as P

eps_value = 1e-06


def normalize(tokens, gain):
    values = tokens.astype(jnp.float32)
    meansq = jnp.mean(values * values, axis=-1, keepdims=True)
    return (values * lax.rsqrt(meansq + eps_value) * gain).astype(jnp.bfloat16)


def gate_dense(expert_ids, gate_values, number):
    labels = jnp.arange(number, dtype=jnp.int32)
    hits = (expert_ids[..., None] == labels).astype(jnp.float32)
    return jnp.sum(hits * gate_values[..., None], axis=-2)


def dispatch_table(column, capacity):
    matched = (column > 0).astype(jnp.float32)
    slots = jnp.cumsum(matched, axis=-1) - 1.0
    places = jnp.arange(capacity).astype(jnp.float32)
    chosen = (slots[..., None, :] == places[:, None]) & (matched[..., None, :] > 0)
    return chosen


def expert_mlp(slot_rows, gate_matrix, up_matrix, down_matrix):
    gated = jnp.dot(slot_rows, gate_matrix, preferred_element_type=jnp.float32)
    upward = jnp.dot(slot_rows, up_matrix, preferred_element_type=jnp.float32)
    hidden = (jax.nn.silu(gated) * upward).astype(jnp.bfloat16)
    return jnp.dot(hidden, down_matrix, preferred_element_type=jnp.float32).astype(jnp.bfloat16)


def bf16_parts(values, count):
    parts = []
    rest = values
    for _ in range(count):
        head = lax.reduce_precision(rest, exponent_bits=8, mantissa_bits=7)
        parts.append(head.astype(jnp.bfloat16))
        rest = rest - head
    return parts


def route(group, move):
    return [(i, move(i)) for i in range(group)]


def local(tokens, gain, expert_ids, gate_values, w_gate, w_up, w_down):
    group = lax.axis_size("expert")
    ring = group // 2
    position = lax.axis_index("expert")
    local_rows, width = tokens.shape
    chosen_count = expert_ids.shape[1]
    number = group * w_gate.shape[0]
    capacity = local_rows * chosen_count // number * 3 // 2
    mine = position

    partner = route(group, lambda i: i ^ 1)
    plus = route(group, lambda i: ((i // 2 + 1) % ring) * 2 + i % 2)
    minus = route(group, lambda i: ((i // 2 - 1) % ring) * 2 + i % 2)

    def send(x, perm):
        return lax.ppermute(x, "expert", perm)

    normed = normalize(tokens, gain)
    dense = gate_dense(expert_ids, gate_values, number)

    tok = {(0, 0): normed, (0, 1): send(normed, partner)}
    den = {(0, 0): dense, (0, 1): send(dense, partner)}
    pair_tok = jnp.stack([tok[(0, 0)], tok[(0, 1)]])
    pair_den = jnp.stack([den[(0, 0)], den[(0, 1)]])
    up_tok, up_den = pair_tok, pair_den
    dn_tok, dn_den = pair_tok, pair_den
    half = ring // 2
    arrivals = [[(0, 0), (0, 1)]]
    for step in range(1, half):
        up_tok, up_den = send(up_tok, plus), send(up_den, plus)
        dn_tok, dn_den = send(dn_tok, minus), send(dn_den, minus)
        for p in range(2):
            tok[(-step, p)], den[(-step, p)] = up_tok[p], up_den[p]
            tok[(step, p)], den[(step, p)] = dn_tok[p], dn_den[p]
        arrivals.append([(-step, 0), (-step, 1), (step, 0), (step, 1)])
    tok[(-half, 0)] = send(up_tok[0], plus)
    den[(-half, 0)] = send(up_den[0], plus)
    tok[(half, 1)] = send(dn_tok[1], minus)
    den[(half, 1)] = send(dn_den[1], minus)
    arrivals.append([(-half, 0), (half, 1)])

    contrib = {}
    for keys in arrivals:
        columns = [lax.dynamic_index_in_dim(den[k], mine, 1, keepdims=False) for k in keys]
        chosen = [dispatch_table(c, capacity) for c in columns]
        rows = [
            jnp.dot(ch.astype(jnp.bfloat16), tok[k], preferred_element_type=jnp.float32)
            for ch, k in zip(chosen, keys)
        ]
        rows = jnp.concatenate(rows, axis=0).astype(jnp.bfloat16)
        out = expert_mlp(rows, w_gate[0], w_up[0], w_down[0])
        for i, k in enumerate(keys):
            block = out[i * capacity:(i + 1) * capacity]
            weights = jnp.where(chosen[i], columns[i][None, :], 0.0)
            total = None
            for part in bf16_parts(weights, 3):
                term = lax.dot_general(
                    part, block, (((0,), (0,)), ((), ())), preferred_element_type=jnp.float32
                )
                total = term if total is None else total + term
            contrib[k] = total

    dn_part = send(contrib[(-half, 0)].astype(jnp.bfloat16), minus)
    up_part = send(contrib[(half, 1)].astype(jnp.bfloat16), plus)
    dn_acc = jnp.stack([dn_part.astype(jnp.float32) + contrib[(-(half - 1), 0)],
                        contrib[(-(half - 1), 1)]])
    up_acc = jnp.stack([contrib[(half - 1, 0)],
                        up_part.astype(jnp.float32) + contrib[(half - 1, 1)]])
    for step in range(half - 1, 0, -1):
        dn_part = send(dn_acc.astype(jnp.bfloat16), minus)
        up_part = send(up_acc.astype(jnp.bfloat16), plus)
        if step > 1:
            dn_acc = dn_part.astype(jnp.float32) + jnp.stack(
                [contrib[(-(step - 1), 0)], contrib[(-(step - 1), 1)]])
            up_acc = up_part.astype(jnp.float32) + jnp.stack(
                [contrib[(step - 1, 0)], contrib[(step - 1, 1)]])
    final = (dn_part.astype(jnp.float32) + up_part.astype(jnp.float32)
             + jnp.stack([contrib[(0, 0)], contrib[(0, 1)]]))
    other = send(final[1].astype(jnp.bfloat16), partner)
    mixed = final[0] + other.astype(jnp.float32)
    return mixed.astype(jnp.bfloat16)


def solution(mesh):
    return jax.shard_map(
        local,
        mesh=mesh,
        in_specs=(
            P(("dp", "expert"), None),
            P(),
            P(("dp", "expert"), None),
            P(("dp", "expert"), None),
            P("expert", None, None),
            P("expert", None, None),
            P("expert", None, None),
        ),
        out_specs=P(("dp", "expert"), None),
        check_vma=False,
    )
```

```python
import jax
import jax.numpy as jnp
from jax import lax
from jax.sharding import PartitionSpec as P

eps_value = 1e-06


def normalize(tokens, gain):
    values = tokens.astype(jnp.float32)
    meansq = jnp.mean(values * values, axis=-1, keepdims=True)
    return (values * lax.rsqrt(meansq + eps_value) * gain).astype(jnp.bfloat16)


def gate_dense(expert_ids, gate_values, number):
    labels = jnp.arange(number, dtype=jnp.int32)
    hits = (expert_ids[..., None] == labels).astype(jnp.float32)
    return jnp.sum(hits * gate_values[..., None], axis=-2)


def dispatch_table(column, capacity):
    matched = (column > 0).astype(jnp.float32)
    slots = jnp.cumsum(matched, axis=-1) - 1.0
    places = jnp.arange(capacity).astype(jnp.float32)
    chosen = (slots[..., None, :] == places[:, None]) & (matched[..., None, :] > 0)
    return chosen


def expert_mlp(slot_rows, gate_matrix, up_matrix, down_matrix):
    gated = jnp.dot(slot_rows, gate_matrix, preferred_element_type=jnp.float32)
    upward = jnp.dot(slot_rows, up_matrix, preferred_element_type=jnp.float32)
    hidden = (jax.nn.silu(gated) * upward).astype(jnp.bfloat16)
    return jnp.dot(hidden, down_matrix, preferred_element_type=jnp.float32).astype(jnp.bfloat16)


def bf16_parts(values, count):
    parts = []
    rest = values
    for _ in range(count):
        head = lax.reduce_precision(rest, exponent_bits=8, mantissa_bits=7)
        parts.append(head.astype(jnp.bfloat16))
        rest = rest - head
    return parts


def route(group, move):
    return [(i, move(i)) for i in range(group)]


def local(tokens, gain, expert_ids, gate_values, w_gate, w_up, w_down):
    group = lax.axis_size("expert")
    ring = group // 2
    position = lax.axis_index("expert")
    local_rows, width = tokens.shape
    chosen_count = expert_ids.shape[1]
    number = group * w_gate.shape[0]
    capacity = local_rows * chosen_count // number * 3 // 2
    mine = position

    partner = route(group, lambda i: i ^ 1)
    plus = route(group, lambda i: ((i // 2 + 1) % ring) * 2 + i % 2)
    minus = route(group, lambda i: ((i // 2 - 1) % ring) * 2 + i % 2)

    def send(x, perm):
        return lax.ppermute(x, "expert", perm)

    normed = normalize(tokens, gain)
    dense = gate_dense(expert_ids, gate_values, number)

    matched = dense > 0
    earlier = (jnp.arange(local_rows)[None, :] <= jnp.arange(local_rows)[:, None])
    rank = jnp.dot(earlier.astype(jnp.bfloat16), matched.astype(jnp.bfloat16),
                   preferred_element_type=jnp.float32)
    code = jnp.where(matched, rank - 1.0, -1.0).astype(jnp.bfloat16)
    meta = [code] + bf16_parts(dense, 3)
    extra = 128
    filler = jnp.zeros((local_rows, extra - len(meta) * number), jnp.bfloat16)
    packed = jnp.concatenate([normed] + meta + [filler], axis=1)

    tok = {(0, 0): packed, (0, 1): send(packed, partner)}
    pair_tok = jnp.stack([tok[(0, 0)], tok[(0, 1)]])
    up_tok = pair_tok
    dn_tok = pair_tok
    half = ring // 2
    arrivals = [[(0, 0), (0, 1)]]
    for step in range(1, half):
        up_tok = send(up_tok, plus)
        dn_tok = send(dn_tok, minus)
        for p in range(2):
            tok[(-step, p)] = up_tok[p]
            tok[(step, p)] = dn_tok[p]
        arrivals.append([(-step, 0), (-step, 1), (step, 0), (step, 1)])
    tok[(-half, 0)] = send(up_tok[0], plus)
    tok[(half, 1)] = send(dn_tok[1], minus)
    arrivals.append([(-half, 0), (half, 1)])

    places = jnp.arange(capacity, dtype=jnp.float32)[:, None]
    contrib = {}
    for keys in arrivals:
        chosen, weights = [], []
        for k in keys:
            info = lax.dynamic_slice_in_dim(tok[k][:, width:], mine, number * len(meta), 1)
            cols = [info[:, j * number].astype(jnp.float32) for j in range(len(meta))]
            hit = cols[0][None, :] == places
            chosen.append(hit)
            weights.append([jnp.where(hit, c[None, :], 0.0).astype(jnp.bfloat16) for c in cols[1:]])
        rows = [
            jnp.dot(ch.astype(jnp.bfloat16), tok[k][:, :width], preferred_element_type=jnp.float32)
            for ch, k in zip(chosen, keys)
        ]
        rows = jnp.concatenate(rows, axis=0).astype(jnp.bfloat16)
        out = expert_mlp(rows, w_gate[0], w_up[0], w_down[0])
        for i, k in enumerate(keys):
            block = out[i * capacity:(i + 1) * capacity]
            total = None
            for part in weights[i]:
                term = lax.dot_general(
                    part, block, (((0,), (0,)), ((), ())), preferred_element_type=jnp.float32
                )
                total = term if total is None else total + term
            contrib[k] = total

    dn_part = send(contrib[(-half, 0)].astype(jnp.bfloat16), minus)
    up_part = send(contrib[(half, 1)].astype(jnp.bfloat16), plus)
    dn_acc = jnp.stack([dn_part.astype(jnp.float32) + contrib[(-(half - 1), 0)],
                        contrib[(-(half - 1), 1)]])
    up_acc = jnp.stack([contrib[(half - 1, 0)],
                        up_part.astype(jnp.float32) + contrib[(half - 1, 1)]])
    for step in range(half - 1, 0, -1):
        dn_part = send(dn_acc.astype(jnp.bfloat16), minus)
        up_part = send(up_acc.astype(jnp.bfloat16), plus)
        if step > 1:
            dn_acc = dn_part.astype(jnp.float32) + jnp.stack(
                [contrib[(-(step - 1), 0)], contrib[(-(step - 1), 1)]])
            up_acc = up_part.astype(jnp.float32) + jnp.stack(
                [contrib[(step - 1, 0)], contrib[(step - 1, 1)]])
    final = (dn_part.astype(jnp.float32) + up_part.astype(jnp.float32)
             + jnp.stack([contrib[(0, 0)], contrib[(0, 1)]]))
    other = send(final[1].astype(jnp.bfloat16), partner)
    mixed = final[0] + other.astype(jnp.float32)
    return mixed.astype(jnp.bfloat16)


def solution(mesh):
    return jax.shard_map(
        local,
        mesh=mesh,
        in_specs=(
            P(("dp", "expert"), None),
            P(),
            P(("dp", "expert"), None),
            P(("dp", "expert"), None),
            P("expert", None, None),
            P("expert", None, None),
            P("expert", None, None),
        ),
        out_specs=P(("dp", "expert"), None),
        check_vma=False,
    )
```

```python
import jax
import jax.numpy as jnp
from jax import lax
from jax.sharding import PartitionSpec as P

eps_value = 1e-06


def normalize(tokens, gain):
    values = tokens.astype(jnp.float32)
    meansq = jnp.mean(values * values, axis=-1, keepdims=True)
    return (values * lax.rsqrt(meansq + eps_value) * gain).astype(jnp.bfloat16)


def gate_dense(expert_ids, gate_values, number):
    labels = jnp.arange(number, dtype=jnp.int32)
    hits = (expert_ids[..., None] == labels).astype(jnp.float32)
    return jnp.sum(hits * gate_values[..., None], axis=-2)


def dispatch_table(column, capacity):
    matched = (column > 0).astype(jnp.float32)
    slots = jnp.cumsum(matched, axis=-1) - 1.0
    places = jnp.arange(capacity).astype(jnp.float32)
    chosen = (slots[..., None, :] == places[:, None]) & (matched[..., None, :] > 0)
    return chosen


def expert_mlp(slot_rows, gate_matrix, up_matrix, down_matrix):
    gated = jnp.dot(slot_rows, gate_matrix, preferred_element_type=jnp.float32)
    upward = jnp.dot(slot_rows, up_matrix, preferred_element_type=jnp.float32)
    hidden = (jax.nn.silu(gated) * upward).astype(jnp.bfloat16)
    return jnp.dot(hidden, down_matrix, preferred_element_type=jnp.float32).astype(jnp.bfloat16)


def bf16_parts(values, count):
    parts = []
    rest = values
    for _ in range(count):
        head = lax.reduce_precision(rest, exponent_bits=8, mantissa_bits=7)
        parts.append(head.astype(jnp.bfloat16))
        rest = rest - head
    return parts


def route(group, move):
    return [(i, move(i)) for i in range(group)]


def local(tokens, gain, expert_ids, gate_values, w_gate, w_up, w_down):
    group = lax.axis_size("expert")
    ring = group // 2
    position = lax.axis_index("expert")
    local_rows, width = tokens.shape
    chosen_count = expert_ids.shape[1]
    number = group * w_gate.shape[0]
    capacity = local_rows * chosen_count // number * 3 // 2
    mine = position

    partner = route(group, lambda i: i ^ 1)
    plus = route(group, lambda i: ((i // 2 + 1) % ring) * 2 + i % 2)
    minus = route(group, lambda i: ((i // 2 - 1) % ring) * 2 + i % 2)

    def send(x, perm):
        return lax.ppermute(x, "expert", perm)

    normed = normalize(tokens, gain)
    dense = gate_dense(expert_ids, gate_values, number)

    matched = dense > 0
    earlier = (jnp.arange(local_rows)[None, :] <= jnp.arange(local_rows)[:, None])
    rank = jnp.dot(earlier.astype(jnp.bfloat16), matched.astype(jnp.bfloat16),
                   preferred_element_type=jnp.float32)
    code = jnp.where(matched, rank - 1.0, -1.0).astype(jnp.bfloat16)
    meta = [code] + bf16_parts(dense, 3)
    extra = 128
    filler = jnp.zeros((local_rows, extra - len(meta) * number), jnp.bfloat16)
    packed = jnp.concatenate([normed] + meta + [filler], axis=1)

    places = jnp.arange(capacity, dtype=jnp.float32)[:, None]

    def process(blocks):
        chosen, weights = [], []
        for block in blocks:
            info = lax.dynamic_slice_in_dim(block[:, width:], mine, number * len(meta), 1)
            cols = [info[:, j * number].astype(jnp.float32) for j in range(len(meta))]
            hit = cols[0][None, :] == places
            chosen.append(hit)
            weights.append([jnp.where(hit, c[None, :], 0.0).astype(jnp.bfloat16)
                            for c in cols[1:3]])
        rows = [
            jnp.dot(ch.astype(jnp.bfloat16), block[:, :width], preferred_element_type=jnp.float32)
            for ch, block in zip(chosen, blocks)
        ]
        rows = jnp.concatenate(rows, axis=0).astype(jnp.bfloat16)
        out = expert_mlp(rows, w_gate[0], w_up[0], w_down[0])
        result = []
        for i in range(len(blocks)):
            part_rows = out[i * capacity:(i + 1) * capacity]
            total = None
            for part in weights[i]:
                term = lax.dot_general(
                    part, part_rows, (((0,), (0,)), ((), ())), preferred_element_type=jnp.float32
                )
                total = term if total is None else total + term
            result.append(total)
        return result

    other = send(packed, partner)
    pair_tok = jnp.stack([packed, other])
    contrib = {}
    queue = [process([packed, other])]
    contrib[(0, 0)], contrib[(0, 1)] = queue[0]
    up_tok = pair_tok
    dn_tok = pair_tok
    half = ring // 2
    for step in range(1, half):
        if step > 1:
            up_tok, dn_tok, _ = lax.optimization_barrier((up_tok, dn_tok, queue.pop(0)))
        up_tok = send(up_tok, plus)
        dn_tok = send(dn_tok, minus)
        queue.append(process([up_tok[0], up_tok[1], dn_tok[0], dn_tok[1]]))
        (contrib[(-step, 0)], contrib[(-step, 1)],
         contrib[(step, 0)], contrib[(step, 1)]) = queue[-1]
    up_last, dn_last, _ = lax.optimization_barrier((up_tok[0], dn_tok[1], queue.pop(0)))
    far = [send(up_last, plus), send(dn_last, minus)]
    far = lax.optimization_barrier((far, queue.pop(0)))[0]
    contrib[(-half, 0)], contrib[(half, 1)] = process(far)

    dn_part = send(contrib[(-half, 0)].astype(jnp.bfloat16), minus)
    up_part = send(contrib[(half, 1)].astype(jnp.bfloat16), plus)
    dn_acc = jnp.stack([dn_part.astype(jnp.float32) + contrib[(-(half - 1), 0)],
                        contrib[(-(half - 1), 1)]])
    up_acc = jnp.stack([contrib[(half - 1, 0)],
                        up_part.astype(jnp.float32) + contrib[(half - 1, 1)]])
    for step in range(half - 1, 0, -1):
        dn_part = send(dn_acc.astype(jnp.bfloat16), minus)
        up_part = send(up_acc.astype(jnp.bfloat16), plus)
        if step > 1:
            dn_acc = dn_part.astype(jnp.float32) + jnp.stack(
                [contrib[(-(step - 1), 0)], contrib[(-(step - 1), 1)]])
            up_acc = up_part.astype(jnp.float32) + jnp.stack(
                [contrib[(step - 1, 0)], contrib[(step - 1, 1)]])
    final = (dn_part.astype(jnp.float32) + up_part.astype(jnp.float32)
             + jnp.stack([contrib[(0, 0)], contrib[(0, 1)]]))
    other = send(final[1].astype(jnp.bfloat16), partner)
    mixed = final[0] + other.astype(jnp.float32)
    return mixed.astype(jnp.bfloat16)


def solution(mesh):
    return jax.shard_map(
        local,
        mesh=mesh,
        in_specs=(
            P(("dp", "expert"), None),
            P(),
            P(("dp", "expert"), None),
            P(("dp", "expert"), None),
            P("expert", None, None),
            P("expert", None, None),
            P("expert", None, None),
        ),
        out_specs=P(("dp", "expert"), None),
        check_vma=False,
    )
```

```python
import jax
import jax.numpy as jnp
from jax import lax
from jax.sharding import PartitionSpec as P

eps_value = 1e-06


def normalize(tokens, gain):
    values = tokens.astype(jnp.float32)
    meansq = jnp.mean(values * values, axis=-1, keepdims=True)
    return (values * lax.rsqrt(meansq + eps_value) * gain).astype(jnp.bfloat16)


def gate_dense(expert_ids, gate_values, number):
    labels = jnp.arange(number, dtype=jnp.int32)
    hits = (expert_ids[..., None] == labels).astype(jnp.float32)
    return jnp.sum(hits * gate_values[..., None], axis=-2)


def dispatch_table(column, capacity):
    matched = (column > 0).astype(jnp.float32)
    slots = jnp.cumsum(matched, axis=-1) - 1.0
    places = jnp.arange(capacity).astype(jnp.float32)
    chosen = (slots[..., None, :] == places[:, None]) & (matched[..., None, :] > 0)
    return chosen


def expert_mlp(slot_rows, gate_matrix, up_matrix, down_matrix):
    gated = jnp.dot(slot_rows, gate_matrix, preferred_element_type=jnp.float32)
    upward = jnp.dot(slot_rows, up_matrix, preferred_element_type=jnp.float32)
    hidden = (jax.nn.silu(gated) * upward).astype(jnp.bfloat16)
    return jnp.dot(hidden, down_matrix, preferred_element_type=jnp.float32).astype(jnp.bfloat16)


def bf16_parts(values, count):
    parts = []
    rest = values
    for _ in range(count):
        head = lax.reduce_precision(rest, exponent_bits=8, mantissa_bits=7)
        parts.append(head.astype(jnp.bfloat16))
        rest = rest - head
    return parts


def route(group, move):
    return [(i, move(i)) for i in range(group)]


def local(tokens, gain, expert_ids, gate_values, w_gate, w_up, w_down):
    group = lax.axis_size("expert")
    ring = group // 2
    position = lax.axis_index("expert")
    local_rows, width = tokens.shape
    chosen_count = expert_ids.shape[1]
    number = group * w_gate.shape[0]
    capacity = local_rows * chosen_count // number * 3 // 2
    mine = position

    partner = route(group, lambda i: i ^ 1)
    plus = route(group, lambda i: ((i // 2 + 1) % ring) * 2 + i % 2)
    minus = route(group, lambda i: ((i // 2 - 1) % ring) * 2 + i % 2)

    def send(x, perm):
        return lax.ppermute(x, "expert", perm)

    normed = normalize(tokens, gain)
    dense = gate_dense(expert_ids, gate_values, number)

    matched = dense > 0
    earlier = (jnp.arange(local_rows)[None, :] <= jnp.arange(local_rows)[:, None])
    rank = jnp.dot(earlier.astype(jnp.bfloat16), matched.astype(jnp.bfloat16),
                   preferred_element_type=jnp.float32)
    code = jnp.where(matched, rank - 1.0, -1.0).astype(jnp.bfloat16)
    meta = [code] + bf16_parts(dense, 3)
    extra = 128
    filler = jnp.zeros((local_rows, extra - len(meta) * number), jnp.bfloat16)
    packed = jnp.concatenate([normed] + meta + [filler], axis=1)

    places = jnp.arange(capacity, dtype=jnp.float32)[:, None]

    def process(blocks):
        chosen, weights = [], []
        for block in blocks:
            info = lax.dynamic_slice_in_dim(block[:, width:], mine, number * len(meta), 1)
            cols = [info[:, j * number].astype(jnp.float32) for j in range(len(meta))]
            hit = cols[0][None, :] == places
            chosen.append(hit)
            weights.append([jnp.where(hit, c[None, :], 0.0).astype(jnp.bfloat16)
                            for c in cols[1:3]])
        rows = [
            jnp.dot(ch.astype(jnp.bfloat16), block[:, :width], preferred_element_type=jnp.float32)
            for ch, block in zip(chosen, blocks)
        ]
        rows = jnp.concatenate(rows, axis=0).astype(jnp.bfloat16)
        out = expert_mlp(rows, w_gate[0], w_up[0], w_down[0])
        result = []
        for i in range(len(blocks)):
            part_rows = out[i * capacity:(i + 1) * capacity]
            total = None
            for part in weights[i]:
                term = lax.dot_general(
                    part, part_rows, (((0,), (0,)), ((), ())), preferred_element_type=jnp.float32
                )
                total = term if total is None else total + term
            result.append(total)
        return result

    other = send(packed, partner)
    pair_tok = jnp.stack([packed, other])
    contrib = {}
    half = ring // 2
    contrib[(0, 0)], contrib[(0, 1)] = process([packed, other])
    done = {0: [contrib[(0, 0)], contrib[(0, 1)]]}
    up_tok = pair_tok
    dn_tok = pair_tok
    arrived = {}
    for step in range(1, half):
        if step > 1:
            up_tok, dn_tok, _ = lax.optimization_barrier((up_tok, dn_tok, done[step - 2]))
        up_tok = send(up_tok, plus)
        dn_tok = send(dn_tok, minus)
        arrived[step] = [up_tok[0], up_tok[1], dn_tok[0], dn_tok[1]]
        if step < half - 2:
            done[step] = process(arrived[step])
    far = [send(up_tok[0], plus), send(dn_tok[1], minus)]
    last = process(arrived[half - 1])
    far = lax.optimization_barrier((far, last))[0]
    ends = process(far)
    late_blocks = lax.optimization_barrier((arrived[half - 2], ends))[0]
    late = process(late_blocks)
    for step, result in [(s, done[s]) for s in range(1, half - 2)] + [(half - 1, last), (half - 2, late)]:
        (contrib[(-step, 0)], contrib[(-step, 1)],
         contrib[(step, 0)], contrib[(step, 1)]) = result
    contrib[(-half, 0)], contrib[(half, 1)] = ends

    dn_part = send(contrib[(-half, 0)].astype(jnp.bfloat16), minus)
    up_part = send(contrib[(half, 1)].astype(jnp.bfloat16), plus)
    dn_acc = jnp.stack([dn_part.astype(jnp.float32) + contrib[(-(half - 1), 0)],
                        contrib[(-(half - 1), 1)]])
    up_acc = jnp.stack([contrib[(half - 1, 0)],
                        up_part.astype(jnp.float32) + contrib[(half - 1, 1)]])
    for step in range(half - 1, 0, -1):
        dn_part = send(dn_acc.astype(jnp.bfloat16), minus)
        up_part = send(up_acc.astype(jnp.bfloat16), plus)
        if step > 1:
            dn_acc = dn_part.astype(jnp.float32) + jnp.stack(
                [contrib[(-(step - 1), 0)], contrib[(-(step - 1), 1)]])
            up_acc = up_part.astype(jnp.float32) + jnp.stack(
                [contrib[(step - 1, 0)], contrib[(step - 1, 1)]])
    final = (dn_part.astype(jnp.float32) + up_part.astype(jnp.float32)
             + jnp.stack([contrib[(0, 0)], contrib[(0, 1)]]))
    other = send(final[1].astype(jnp.bfloat16), partner)
    mixed = final[0] + other.astype(jnp.float32)
    return mixed.astype(jnp.bfloat16)


def solution(mesh):
    return jax.shard_map(
        local,
        mesh=mesh,
        in_specs=(
            P(("dp", "expert"), None),
            P(),
            P(("dp", "expert"), None),
            P(("dp", "expert"), None),
            P("expert", None, None),
            P("expert", None, None),
            P("expert", None, None),
        ),
        out_specs=P(("dp", "expert"), None),
        check_vma=False,
    )
```

```python
import jax
import jax.numpy as jnp
from jax import lax
from jax.sharding import PartitionSpec as P

eps_value = 1e-06


def normalize(tokens, gain):
    values = tokens.astype(jnp.float32)
    meansq = jnp.mean(values * values, axis=-1, keepdims=True)
    return (values * lax.rsqrt(meansq + eps_value) * gain).astype(jnp.bfloat16)


def gate_dense(expert_ids, gate_values, number):
    labels = jnp.arange(number, dtype=jnp.int32)
    hits = (expert_ids[..., None] == labels).astype(jnp.float32)
    return jnp.sum(hits * gate_values[..., None], axis=-2)


def dispatch_table(column, capacity):
    matched = (column > 0).astype(jnp.float32)
    slots = jnp.cumsum(matched, axis=-1) - 1.0
    places = jnp.arange(capacity).astype(jnp.float32)
    chosen = (slots[..., None, :] == places[:, None]) & (matched[..., None, :] > 0)
    return chosen


def expert_mlp(slot_rows, gate_matrix, up_matrix, down_matrix):
    gated = jnp.dot(slot_rows, gate_matrix, preferred_element_type=jnp.float32)
    upward = jnp.dot(slot_rows, up_matrix, preferred_element_type=jnp.float32)
    hidden = (jax.nn.silu(gated) * upward).astype(jnp.bfloat16)
    return jnp.dot(hidden, down_matrix, preferred_element_type=jnp.float32).astype(jnp.bfloat16)


def bf16_parts(values, count):
    parts = []
    rest = values
    for _ in range(count):
        head = lax.reduce_precision(rest, exponent_bits=8, mantissa_bits=7)
        parts.append(head.astype(jnp.bfloat16))
        rest = rest - head
    return parts


def route(group, move):
    return [(i, move(i)) for i in range(group)]


def local(tokens, gain, expert_ids, gate_values, w_gate, w_up, w_down):
    group = lax.axis_size("expert")
    ring = group // 2
    position = lax.axis_index("expert")
    local_rows, width = tokens.shape
    chosen_count = expert_ids.shape[1]
    number = group * w_gate.shape[0]
    capacity = local_rows * chosen_count // number * 3 // 2
    mine = position

    partner = route(group, lambda i: i ^ 1)
    plus = route(group, lambda i: ((i // 2 + 1) % ring) * 2 + i % 2)
    minus = route(group, lambda i: ((i // 2 - 1) % ring) * 2 + i % 2)

    def send(x, perm):
        return lax.ppermute(x, "expert", perm)

    normed = normalize(tokens, gain)
    dense = gate_dense(expert_ids, gate_values, number)

    matched = dense > 0
    earlier = (jnp.arange(local_rows)[None, :] <= jnp.arange(local_rows)[:, None])
    rank = jnp.dot(earlier.astype(jnp.bfloat16), matched.astype(jnp.bfloat16),
                   preferred_element_type=jnp.float32)
    code = jnp.where(matched, rank - 1.0, -1.0).astype(jnp.bfloat16)
    meta = [code] + bf16_parts(dense, 3)
    extra = 128
    filler = jnp.zeros((local_rows, extra - len(meta) * number), jnp.bfloat16)
    packed = jnp.concatenate([normed] + meta + [filler], axis=1)

    places = jnp.arange(capacity, dtype=jnp.float32)[:, None]

    def process(blocks):
        chosen, weights = [], []
        for block in blocks:
            info = lax.dynamic_slice_in_dim(block[:, width:], mine, number * len(meta), 1)
            cols = [info[:, j * number].astype(jnp.float32) for j in range(len(meta))]
            hit = cols[0][None, :] == places
            chosen.append(hit)
            weights.append([jnp.where(hit, c[None, :], 0.0).astype(jnp.bfloat16)
                            for c in cols[1:3]])
        rows = [
            jnp.dot(ch.astype(jnp.bfloat16), block[:, :width], preferred_element_type=jnp.float32)
            for ch, block in zip(chosen, blocks)
        ]
        rows = jnp.concatenate(rows, axis=0).astype(jnp.bfloat16)
        out = expert_mlp(rows, w_gate[0], w_up[0], w_down[0])
        result = []
        for i in range(len(blocks)):
            part_rows = out[i * capacity:(i + 1) * capacity]
            total = None
            for part in weights[i]:
                term = lax.dot_general(
                    part, part_rows, (((0,), (0,)), ((), ())), preferred_element_type=jnp.float32
                )
                total = term if total is None else total + term
            result.append(total)
        return result

    other = send(packed, partner)
    pair_tok = jnp.stack([packed, other])
    contrib = {}
    half = ring // 2
    contrib[(0, 0)], contrib[(0, 1)] = process([packed, other])
    done = {0: [contrib[(0, 0)], contrib[(0, 1)]]}
    up_tok = pair_tok
    dn_tok = pair_tok
    arrived = {}
    for step in range(1, half):
        if step > 1:
            up_tok, dn_tok, _ = lax.optimization_barrier((up_tok, dn_tok, done[step - 2]))
        up_tok = send(up_tok, plus)
        dn_tok = send(dn_tok, minus)
        arrived[step] = [up_tok[0], up_tok[1], dn_tok[0], dn_tok[1]]
        if step < half - 2:
            done[step] = process(arrived[step])
    far = [send(up_tok[0], plus), send(dn_tok[1], minus)]
    last = process(arrived[half - 1])
    far = lax.optimization_barrier((far, last))[0]
    ends = process(far[:1])
    far_other = lax.optimization_barrier((far[1], ends))[0]
    ends = ends + process([far_other])
    late_blocks = lax.optimization_barrier((arrived[half - 2], ends))[0]
    late = process(late_blocks)
    for step, result in [(s, done[s]) for s in range(1, half - 2)] + [(half - 1, last), (half - 2, late)]:
        (contrib[(-step, 0)], contrib[(-step, 1)],
         contrib[(step, 0)], contrib[(step, 1)]) = result
    contrib[(-half, 0)], contrib[(half, 1)] = ends

    dn_part = send(contrib[(-half, 0)].astype(jnp.bfloat16), minus)
    up_part = send(contrib[(half, 1)].astype(jnp.bfloat16), plus)
    dn_acc = jnp.stack([dn_part.astype(jnp.float32) + contrib[(-(half - 1), 0)],
                        contrib[(-(half - 1), 1)]])
    up_acc = jnp.stack([contrib[(half - 1, 0)],
                        up_part.astype(jnp.float32) + contrib[(half - 1, 1)]])
    for step in range(half - 1, 0, -1):
        dn_part = send(dn_acc.astype(jnp.bfloat16), minus)
        up_part = send(up_acc.astype(jnp.bfloat16), plus)
        if step > 1:
            dn_acc = dn_part.astype(jnp.float32) + jnp.stack(
                [contrib[(-(step - 1), 0)], contrib[(-(step - 1), 1)]])
            up_acc = up_part.astype(jnp.float32) + jnp.stack(
                [contrib[(step - 1, 0)], contrib[(step - 1, 1)]])
    final = (dn_part.astype(jnp.float32) + up_part.astype(jnp.float32)
             + jnp.stack([contrib[(0, 0)], contrib[(0, 1)]]))
    other = send(final[1].astype(jnp.bfloat16), partner)
    mixed = final[0] + other.astype(jnp.float32)
    return mixed.astype(jnp.bfloat16)


def solution(mesh):
    return jax.shard_map(
        local,
        mesh=mesh,
        in_specs=(
            P(("dp", "expert"), None),
            P(),
            P(("dp", "expert"), None),
            P(("dp", "expert"), None),
            P("expert", None, None),
            P("expert", None, None),
            P("expert", None, None),
        ),
        out_specs=P(("dp", "expert"), None),
        check_vma=False,
    )
```

```python
import jax
import jax.numpy as jnp
from jax import lax
from jax.sharding import PartitionSpec as P

eps_value = 1e-06


def normalize(tokens, gain):
    values = tokens.astype(jnp.float32)
    meansq = jnp.mean(values * values, axis=-1, keepdims=True)
    return (values * lax.rsqrt(meansq + eps_value) * gain).astype(jnp.bfloat16)


def gate_dense(expert_ids, gate_values, number):
    labels = jnp.arange(number, dtype=jnp.int32)
    hits = (expert_ids[..., None] == labels).astype(jnp.float32)
    return jnp.sum(hits * gate_values[..., None], axis=-2)


def dispatch_table(column, capacity):
    matched = (column > 0).astype(jnp.float32)
    slots = jnp.cumsum(matched, axis=-1) - 1.0
    places = jnp.arange(capacity).astype(jnp.float32)
    chosen = (slots[..., None, :] == places[:, None]) & (matched[..., None, :] > 0)
    return chosen


def expert_mlp(slot_rows, gate_matrix, up_matrix, down_matrix):
    gated = jnp.dot(slot_rows, gate_matrix, preferred_element_type=jnp.float32)
    upward = jnp.dot(slot_rows, up_matrix, preferred_element_type=jnp.float32)
    hidden = (jax.nn.silu(gated) * upward).astype(jnp.bfloat16)
    return jnp.dot(hidden, down_matrix, preferred_element_type=jnp.float32).astype(jnp.bfloat16)


def bf16_parts(values, count):
    parts = []
    rest = values
    for _ in range(count):
        head = lax.reduce_precision(rest, exponent_bits=8, mantissa_bits=7)
        parts.append(head.astype(jnp.bfloat16))
        rest = rest - head
    return parts


def route(group, move):
    return [(i, move(i)) for i in range(group)]


def local(tokens, gain, expert_ids, gate_values, w_gate, w_up, w_down):
    group = lax.axis_size("expert")
    ring = group // 2
    position = lax.axis_index("expert")
    local_rows, width = tokens.shape
    chosen_count = expert_ids.shape[1]
    number = group * w_gate.shape[0]
    capacity = local_rows * chosen_count // number * 3 // 2
    mine = position

    partner = route(group, lambda i: i ^ 1)
    plus = route(group, lambda i: ((i // 2 + 1) % ring) * 2 + i % 2)
    minus = route(group, lambda i: ((i // 2 - 1) % ring) * 2 + i % 2)

    def send(x, perm):
        return lax.ppermute(x, "expert", perm)

    normed = normalize(tokens, gain)
    dense = gate_dense(expert_ids, gate_values, number)

    matched = dense > 0
    earlier = (jnp.arange(local_rows)[None, :] <= jnp.arange(local_rows)[:, None])
    rank = jnp.dot(earlier.astype(jnp.bfloat16), matched.astype(jnp.bfloat16),
                   preferred_element_type=jnp.float32)
    code = jnp.where(matched, rank - 1.0, -1.0).astype(jnp.bfloat16)
    meta = [code] + bf16_parts(dense, 3)
    extra = 128
    filler = jnp.zeros((local_rows, extra - len(meta) * number), jnp.bfloat16)
    packed = jnp.concatenate([normed] + meta + [filler], axis=1)

    places = jnp.arange(capacity, dtype=jnp.float32)[:, None]

    def process(blocks):
        chosen, scales = [], []
        for block in blocks:
            info = lax.dynamic_slice_in_dim(block[:, width:], mine, number * len(meta), 1)
            cols = [info[:, j * number].astype(jnp.float32) for j in range(len(meta))]
            hit = cols[0][None, :] == places
            gate = (cols[1] + cols[2]) + cols[3]
            chosen.append(hit.astype(jnp.bfloat16))
            scales.append(jnp.sum(jnp.where(hit, gate[None, :], 0.0), axis=1))
        rows = [
            jnp.dot(ch, block[:, :width], preferred_element_type=jnp.float32)
            for ch, block in zip(chosen, blocks)
        ]
        rows = jnp.concatenate(rows, axis=0).astype(jnp.bfloat16)
        gated = jnp.dot(rows, w_gate[0], preferred_element_type=jnp.float32)
        upward = jnp.dot(rows, w_up[0], preferred_element_type=jnp.float32)
        hidden = (jax.nn.silu(gated) * upward).astype(jnp.bfloat16)
        out = jnp.dot(hidden, w_down[0], preferred_element_type=jnp.float32)
        out = (out * jnp.concatenate(scales)[:, None]).astype(jnp.bfloat16)
        result = []
        for i in range(len(blocks)):
            part_rows = out[i * capacity:(i + 1) * capacity]
            result.append(lax.dot_general(
                chosen[i], part_rows, (((0,), (0,)), ((), ())), preferred_element_type=jnp.float32
            ))
        return result

    other = send(packed, partner)
    pair_tok = jnp.stack([packed, other])
    contrib = {}
    half = ring // 2
    contrib[(0, 0)], contrib[(0, 1)] = process([packed, other])
    done = {0: [contrib[(0, 0)], contrib[(0, 1)]]}
    up_tok = pair_tok
    dn_tok = pair_tok
    arrived = {}
    for step in range(1, half):
        if step > 1:
            up_tok, dn_tok, _ = lax.optimization_barrier((up_tok, dn_tok, done[step - 2]))
        up_tok = send(up_tok, plus)
        dn_tok = send(dn_tok, minus)
        arrived[step] = [up_tok[0], up_tok[1], dn_tok[0], dn_tok[1]]
        if step < half - 2:
            done[step] = process(arrived[step])
    far = [send(up_tok[0], plus), send(dn_tok[1], minus)]
    last = process(arrived[half - 1])
    far = lax.optimization_barrier((far, last))[0]
    ends = process(far[:1])
    far_other = lax.optimization_barrier((far[1], ends))[0]
    ends = ends + process([far_other])
    late_blocks = lax.optimization_barrier((arrived[half - 2], ends))[0]
    late = process(late_blocks)
    for step, result in [(s, done[s]) for s in range(1, half - 2)] + [(half - 1, last), (half - 2, late)]:
        (contrib[(-step, 0)], contrib[(-step, 1)],
         contrib[(step, 0)], contrib[(step, 1)]) = result
    contrib[(-half, 0)], contrib[(half, 1)] = ends

    dn_part = send(contrib[(-half, 0)].astype(jnp.bfloat16), minus)
    up_part = send(contrib[(half, 1)].astype(jnp.bfloat16), plus)
    dn_acc = jnp.stack([dn_part.astype(jnp.float32) + contrib[(-(half - 1), 0)],
                        contrib[(-(half - 1), 1)]])
    up_acc = jnp.stack([contrib[(half - 1, 0)],
                        up_part.astype(jnp.float32) + contrib[(half - 1, 1)]])
    for step in range(half - 1, 0, -1):
        dn_part = send(dn_acc.astype(jnp.bfloat16), minus)
        up_part = send(up_acc.astype(jnp.bfloat16), plus)
        if step > 1:
            dn_acc = dn_part.astype(jnp.float32) + jnp.stack(
                [contrib[(-(step - 1), 0)], contrib[(-(step - 1), 1)]])
            up_acc = up_part.astype(jnp.float32) + jnp.stack(
                [contrib[(step - 1, 0)], contrib[(step - 1, 1)]])
    final = (dn_part.astype(jnp.float32) + up_part.astype(jnp.float32)
             + jnp.stack([contrib[(0, 0)], contrib[(0, 1)]]))
    other = send(final[1].astype(jnp.bfloat16), partner)
    mixed = final[0] + other.astype(jnp.float32)
    return mixed.astype(jnp.bfloat16)


def solution(mesh):
    return jax.shard_map(
        local,
        mesh=mesh,
        in_specs=(
            P(("dp", "expert"), None),
            P(),
            P(("dp", "expert"), None),
            P(("dp", "expert"), None),
            P("expert", None, None),
            P("expert", None, None),
            P("expert", None, None),
        ),
        out_specs=P(("dp", "expert"), None),
        check_vma=False,
    )
```

```python
import jax
import jax.numpy as jnp
from jax import lax
from jax.sharding import PartitionSpec as P

eps_value = 1e-06


def normalize(tokens, gain):
    values = tokens.astype(jnp.float32)
    meansq = jnp.mean(values * values, axis=-1, keepdims=True)
    return (values * lax.rsqrt(meansq + eps_value) * gain).astype(jnp.bfloat16)


def gate_dense(expert_ids, gate_values, number):
    labels = jnp.arange(number, dtype=jnp.int32)
    hits = (expert_ids[..., None] == labels).astype(jnp.float32)
    return jnp.sum(hits * gate_values[..., None], axis=-2)


def dispatch_table(column, capacity):
    matched = (column > 0).astype(jnp.float32)
    slots = jnp.cumsum(matched, axis=-1) - 1.0
    places = jnp.arange(capacity).astype(jnp.float32)
    chosen = (slots[..., None, :] == places[:, None]) & (matched[..., None, :] > 0)
    return chosen


def expert_mlp(slot_rows, gate_matrix, up_matrix, down_matrix):
    gated = jnp.dot(slot_rows, gate_matrix, preferred_element_type=jnp.float32)
    upward = jnp.dot(slot_rows, up_matrix, preferred_element_type=jnp.float32)
    hidden = (jax.nn.silu(gated) * upward).astype(jnp.bfloat16)
    return jnp.dot(hidden, down_matrix, preferred_element_type=jnp.float32).astype(jnp.bfloat16)


def bf16_parts(values, count):
    parts = []
    rest = values
    for _ in range(count):
        head = lax.reduce_precision(rest, exponent_bits=8, mantissa_bits=7)
        parts.append(head.astype(jnp.bfloat16))
        rest = rest - head
    return parts


def route(group, move):
    return [(i, move(i)) for i in range(group)]


def local(tokens, gain, expert_ids, gate_values, w_gate, w_up, w_down):
    group = lax.axis_size("expert")
    ring = group // 2
    position = lax.axis_index("expert")
    local_rows, width = tokens.shape
    chosen_count = expert_ids.shape[1]
    number = group * w_gate.shape[0]
    capacity = local_rows * chosen_count // number * 3 // 2
    mine = position

    partner = route(group, lambda i: i ^ 1)
    plus = route(group, lambda i: ((i // 2 + 1) % ring) * 2 + i % 2)
    minus = route(group, lambda i: ((i // 2 - 1) % ring) * 2 + i % 2)

    def send(x, perm):
        return lax.ppermute(x, "expert", perm)

    normed = normalize(tokens, gain)
    dense = gate_dense(expert_ids, gate_values, number)

    matched = dense > 0
    earlier = (jnp.arange(local_rows)[None, :] <= jnp.arange(local_rows)[:, None])
    rank = jnp.dot(earlier.astype(jnp.bfloat16), matched.astype(jnp.bfloat16),
                   preferred_element_type=jnp.float32)
    code = jnp.where(matched, rank - 1.0, -1.0).astype(jnp.bfloat16)
    meta = [code] + bf16_parts(dense, 3)
    extra = 128
    filler = jnp.zeros((local_rows, extra - len(meta) * number), jnp.bfloat16)
    packed = jnp.concatenate([normed] + meta + [filler], axis=1)

    places = jnp.arange(capacity, dtype=jnp.float32)[:, None]

    def process(blocks):
        chosen, scales = [], []
        for block in blocks:
            info = lax.dynamic_slice_in_dim(block[:, width:], mine, number * len(meta), 1)
            cols = [info[:, j * number].astype(jnp.float32) for j in range(len(meta))]
            hit = cols[0][None, :] == places
            gate = (cols[1] + cols[2]) + cols[3]
            chosen.append(hit.astype(jnp.bfloat16))
            scales.append(jnp.sum(jnp.where(hit, gate[None, :], 0.0), axis=1))
        rows = [
            jnp.dot(ch, block[:, :width], preferred_element_type=jnp.float32)
            for ch, block in zip(chosen, blocks)
        ]
        rows = jnp.concatenate(rows, axis=0).astype(jnp.bfloat16)
        gated = jnp.dot(rows, w_gate[0], preferred_element_type=jnp.float32)
        upward = jnp.dot(rows, w_up[0], preferred_element_type=jnp.float32)
        hidden = (jax.nn.silu(gated) * upward).astype(jnp.bfloat16)
        out = jnp.dot(hidden, w_down[0], preferred_element_type=jnp.float32)
        out = (out * jnp.concatenate(scales)[:, None]).astype(jnp.bfloat16)
        result = []
        for i in range(len(blocks)):
            part_rows = out[i * capacity:(i + 1) * capacity]
            result.append(lax.dot_general(
                chosen[i], part_rows, (((0,), (0,)), ((), ())), preferred_element_type=jnp.float32
            ))
        return result

    other = send(packed, partner)
    pair_tok = jnp.stack([packed, other])
    contrib = {}
    half = ring // 2
    contrib[(0, 0)], contrib[(0, 1)] = process([packed, other])
    done = {0: [contrib[(0, 0)], contrib[(0, 1)]]}
    up_tok = pair_tok
    dn_tok = pair_tok
    arrived = {}
    for step in range(1, half):
        if step > 1:
            up_tok, dn_tok, _ = lax.optimization_barrier((up_tok, dn_tok, done[step - 2]))
        up_tok = send(up_tok, plus)
        dn_tok = send(dn_tok, minus)
        arrived[step] = [up_tok[0], up_tok[1], dn_tok[0], dn_tok[1]]
        if step < half - 2:
            done[step] = process(arrived[step])
    far = [send(up_tok[0], plus), send(dn_tok[1], minus)]
    ends = process(far[:1])
    far_other = lax.optimization_barrier((far[1], ends))[0]
    ends = ends + process([far_other])
    last_blocks = lax.optimization_barrier((arrived[half - 1], ends))[0]
    last = process(last_blocks)
    for step, result in [(s, done[s]) for s in range(1, half - 2)] + [(half - 1, last)]:
        (contrib[(-step, 0)], contrib[(-step, 1)],
         contrib[(step, 0)], contrib[(step, 1)]) = result
    contrib[(-half, 0)], contrib[(half, 1)] = ends

    dn_part = send(contrib[(-half, 0)].astype(jnp.bfloat16), minus)
    up_part = send(contrib[(half, 1)].astype(jnp.bfloat16), plus)
    late_blocks, dn_part, up_part = lax.optimization_barrier((arrived[half - 2], dn_part, up_part))
    step = half - 2
    (contrib[(-step, 0)], contrib[(-step, 1)],
     contrib[(step, 0)], contrib[(step, 1)]) = process(late_blocks)
    dn_acc = jnp.stack([dn_part.astype(jnp.float32) + contrib[(-(half - 1), 0)],
                        contrib[(-(half - 1), 1)]])
    up_acc = jnp.stack([contrib[(half - 1, 0)],
                        up_part.astype(jnp.float32) + contrib[(half - 1, 1)]])
    for step in range(half - 1, 0, -1):
        dn_part = send(dn_acc.astype(jnp.bfloat16), minus)
        up_part = send(up_acc.astype(jnp.bfloat16), plus)
        if step > 1:
            dn_acc = dn_part.astype(jnp.float32) + jnp.stack(
                [contrib[(-(step - 1), 0)], contrib[(-(step - 1), 1)]])
            up_acc = up_part.astype(jnp.float32) + jnp.stack(
                [contrib[(step - 1, 0)], contrib[(step - 1, 1)]])
    final = (dn_part.astype(jnp.float32) + up_part.astype(jnp.float32)
             + jnp.stack([contrib[(0, 0)], contrib[(0, 1)]]))
    other = send(final[1].astype(jnp.bfloat16), partner)
    mixed = final[0] + other.astype(jnp.float32)
    return mixed.astype(jnp.bfloat16)


def solution(mesh):
    return jax.shard_map(
        local,
        mesh=mesh,
        in_specs=(
            P(("dp", "expert"), None),
            P(),
            P(("dp", "expert"), None),
            P(("dp", "expert"), None),
            P("expert", None, None),
            P("expert", None, None),
            P("expert", None, None),
        ),
        out_specs=P(("dp", "expert"), None),
        check_vma=False,
    )
```

```python
import jax
import jax.numpy as jnp
from jax import lax
from jax.sharding import PartitionSpec as P

eps_value = 1e-06


def normalize(tokens, gain):
    values = tokens.astype(jnp.float32)
    meansq = jnp.mean(values * values, axis=-1, keepdims=True)
    return (values * lax.rsqrt(meansq + eps_value) * gain).astype(jnp.bfloat16)


def gate_dense(expert_ids, gate_values, number):
    labels = jnp.arange(number, dtype=jnp.int32)
    hits = (expert_ids[..., None] == labels).astype(jnp.float32)
    return jnp.sum(hits * gate_values[..., None], axis=-2)


def dispatch_table(column, capacity):
    matched = (column > 0).astype(jnp.float32)
    slots = jnp.cumsum(matched, axis=-1) - 1.0
    places = jnp.arange(capacity).astype(jnp.float32)
    chosen = (slots[..., None, :] == places[:, None]) & (matched[..., None, :] > 0)
    return chosen


def expert_mlp(slot_rows, gate_matrix, up_matrix, down_matrix):
    gated = jnp.dot(slot_rows, gate_matrix, preferred_element_type=jnp.float32)
    upward = jnp.dot(slot_rows, up_matrix, preferred_element_type=jnp.float32)
    hidden = (jax.nn.silu(gated) * upward).astype(jnp.bfloat16)
    return jnp.dot(hidden, down_matrix, preferred_element_type=jnp.float32).astype(jnp.bfloat16)


def bf16_parts(values, count):
    parts = []
    rest = values
    for _ in range(count):
        head = lax.reduce_precision(rest, exponent_bits=8, mantissa_bits=7)
        parts.append(head.astype(jnp.bfloat16))
        rest = rest - head
    return parts


def route(group, move):
    return [(i, move(i)) for i in range(group)]


def local(tokens, gain, expert_ids, gate_values, w_gate, w_up, w_down):
    group = lax.axis_size("expert")
    ring = group // 2
    position = lax.axis_index("expert")
    local_rows, width = tokens.shape
    chosen_count = expert_ids.shape[1]
    number = group * w_gate.shape[0]
    capacity = local_rows * chosen_count // number * 3 // 2
    mine = position

    partner = route(group, lambda i: i ^ 1)
    plus = route(group, lambda i: ((i // 2 + 1) % ring) * 2 + i % 2)
    minus = route(group, lambda i: ((i // 2 - 1) % ring) * 2 + i % 2)

    def send(x, perm):
        return lax.ppermute(x, "expert", perm)

    normed = normalize(tokens, gain)
    dense = gate_dense(expert_ids, gate_values, number)

    matched = dense > 0
    earlier = (jnp.arange(local_rows)[None, :] <= jnp.arange(local_rows)[:, None])
    rank = jnp.dot(earlier.astype(jnp.bfloat16), matched.astype(jnp.bfloat16),
                   preferred_element_type=jnp.float32)
    code = jnp.where(matched, rank - 1.0, -1.0).astype(jnp.bfloat16)
    meta = [code] + bf16_parts(dense, 3)
    extra = 128
    filler = jnp.zeros((local_rows, extra - len(meta) * number), jnp.bfloat16)
    packed = jnp.concatenate([normed] + meta + [filler], axis=1)

    places = jnp.arange(capacity, dtype=jnp.float32)[:, None]

    def process(blocks):
        chosen, scales = [], []
        for block in blocks:
            info = lax.dynamic_slice_in_dim(block[:, width:], mine, number * len(meta), 1)
            cols = [info[:, j * number].astype(jnp.float32) for j in range(len(meta))]
            hit = cols[0][None, :] == places
            gate = (cols[1] + cols[2]) + cols[3]
            chosen.append(hit.astype(jnp.bfloat16))
            scales.append(jnp.sum(jnp.where(hit, gate[None, :], 0.0), axis=1))
        rows = [
            jnp.dot(ch, block[:, :width], preferred_element_type=jnp.float32)
            for ch, block in zip(chosen, blocks)
        ]
        rows = jnp.concatenate(rows, axis=0).astype(jnp.bfloat16)
        gated = jnp.dot(rows, w_gate[0], preferred_element_type=jnp.float32)
        upward = jnp.dot(rows, w_up[0], preferred_element_type=jnp.float32)
        hidden = (jax.nn.silu(gated) * upward).astype(jnp.bfloat16)
        out = jnp.dot(hidden, w_down[0], preferred_element_type=jnp.float32)
        out = (out * jnp.concatenate(scales)[:, None]).astype(jnp.bfloat16)
        result = []
        for i in range(len(blocks)):
            part_rows = out[i * capacity:(i + 1) * capacity]
            result.append(lax.dot_general(
                chosen[i], part_rows, (((0,), (0,)), ((), ())), preferred_element_type=jnp.float32
            ))
        return result

    other = send(packed, partner)
    contrib = {}
    half = ring // 2
    contrib[(0, 0)], = process([packed])
    done = {0: [contrib[(0, 0)]]}
    up_tok = [packed, other]
    dn_tok = [packed, other]
    arrived = {}
    for step in range(1, half):
        if step > 1:
            up_tok, dn_tok, _ = lax.optimization_barrier((up_tok, dn_tok, done[step - 2]))
        up_tok = [send(x, plus) for x in up_tok]
        dn_tok = [send(x, minus) for x in dn_tok]
        arrived[step] = [up_tok[0], up_tok[1], dn_tok[0], dn_tok[1]]
        if step < half - 2:
            done[step] = process(arrived[step])
    far = [send(up_tok[0], plus), send(dn_tok[1], minus)]
    ends = process(far[:1])
    far_other = lax.optimization_barrier((far[1], ends))[0]
    ends = ends + process([far_other])
    last_blocks = lax.optimization_barrier((arrived[half - 1], ends))[0]
    last = process(last_blocks)
    for step, result in [(s, done[s]) for s in range(1, half - 2)] + [(half - 1, last)]:
        (contrib[(-step, 0)], contrib[(-step, 1)],
         contrib[(step, 0)], contrib[(step, 1)]) = result
    contrib[(-half, 0)], contrib[(half, 1)] = ends

    dn_part = send(contrib[(-half, 0)].astype(jnp.bfloat16), minus)
    up_part = send(contrib[(half, 1)].astype(jnp.bfloat16), plus)
    late_blocks, dn_part, up_part = lax.optimization_barrier((arrived[half - 2], dn_part, up_part))
    step = half - 2
    (contrib[(-step, 0)], contrib[(-step, 1)],
     contrib[(step, 0)], contrib[(step, 1)]) = process(late_blocks)
    dn_acc = jnp.stack([dn_part.astype(jnp.float32) + contrib[(-(half - 1), 0)],
                        contrib[(-(half - 1), 1)]])
    up_acc = jnp.stack([contrib[(half - 1, 0)],
                        up_part.astype(jnp.float32) + contrib[(half - 1, 1)]])
    for step in range(half - 1, 0, -1):
        if step == 1:
            other_late, dn_acc, up_acc = lax.optimization_barrier((other, dn_acc, up_acc))
            contrib[(0, 1)], = process([other_late])
        dn_part = send(dn_acc.astype(jnp.bfloat16), minus)
        up_part = send(up_acc.astype(jnp.bfloat16), plus)
        if step > 1:
            dn_acc = dn_part.astype(jnp.float32) + jnp.stack(
                [contrib[(-(step - 1), 0)], contrib[(-(step - 1), 1)]])
            up_acc = up_part.astype(jnp.float32) + jnp.stack(
                [contrib[(step - 1, 0)], contrib[(step - 1, 1)]])
    final = (dn_part.astype(jnp.float32) + up_part.astype(jnp.float32)
             + jnp.stack([contrib[(0, 0)], contrib[(0, 1)]]))
    other = send(final[1].astype(jnp.bfloat16), partner)
    mixed = final[0] + other.astype(jnp.float32)
    return mixed.astype(jnp.bfloat16)


def solution(mesh):
    return jax.shard_map(
        local,
        mesh=mesh,
        in_specs=(
            P(("dp", "expert"), None),
            P(),
            P(("dp", "expert"), None),
            P(("dp", "expert"), None),
            P("expert", None, None),
            P("expert", None, None),
            P("expert", None, None),
        ),
        out_specs=P(("dp", "expert"), None),
        check_vma=False,
    )
```

```python
import jax
import jax.numpy as jnp
from jax import lax
from jax.sharding import PartitionSpec as P

eps_value = 1e-06


def normalize(tokens, gain):
    values = tokens.astype(jnp.float32)
    meansq = jnp.mean(values * values, axis=-1, keepdims=True)
    return (values * lax.rsqrt(meansq + eps_value) * gain).astype(jnp.bfloat16)


def gate_dense(expert_ids, gate_values, number):
    labels = jnp.arange(number, dtype=jnp.int32)
    hits = (expert_ids[..., None] == labels).astype(jnp.float32)
    return jnp.sum(hits * gate_values[..., None], axis=-2)


def dispatch_table(column, capacity):
    matched = (column > 0).astype(jnp.float32)
    slots = jnp.cumsum(matched, axis=-1) - 1.0
    places = jnp.arange(capacity).astype(jnp.float32)
    chosen = (slots[..., None, :] == places[:, None]) & (matched[..., None, :] > 0)
    return chosen


def expert_mlp(slot_rows, gate_matrix, up_matrix, down_matrix):
    gated = jnp.dot(slot_rows, gate_matrix, preferred_element_type=jnp.float32)
    upward = jnp.dot(slot_rows, up_matrix, preferred_element_type=jnp.float32)
    hidden = (jax.nn.silu(gated) * upward).astype(jnp.bfloat16)
    return jnp.dot(hidden, down_matrix, preferred_element_type=jnp.float32).astype(jnp.bfloat16)


def bf16_parts(values, count):
    parts = []
    rest = values
    for _ in range(count):
        head = lax.reduce_precision(rest, exponent_bits=8, mantissa_bits=7)
        parts.append(head.astype(jnp.bfloat16))
        rest = rest - head
    return parts


def route(group, move):
    return [(i, move(i)) for i in range(group)]


def local(tokens, gain, expert_ids, gate_values, w_gate, w_up, w_down):
    group = lax.axis_size("expert")
    ring = group // 2
    position = lax.axis_index("expert")
    local_rows, width = tokens.shape
    chosen_count = expert_ids.shape[1]
    number = group * w_gate.shape[0]
    capacity = local_rows * chosen_count // number * 3 // 2
    mine = position

    partner = route(group, lambda i: i ^ 1)
    plus = route(group, lambda i: ((i // 2 + 1) % ring) * 2 + i % 2)
    minus = route(group, lambda i: ((i // 2 - 1) % ring) * 2 + i % 2)

    def send(x, perm):
        return lax.ppermute(x, "expert", perm)

    normed = normalize(tokens, gain)
    dense = gate_dense(expert_ids, gate_values, number)

    matched = dense > 0
    earlier = (jnp.arange(local_rows)[None, :] <= jnp.arange(local_rows)[:, None])
    rank = jnp.dot(earlier.astype(jnp.bfloat16), matched.astype(jnp.bfloat16),
                   preferred_element_type=jnp.float32)
    code = jnp.where(matched, rank - 1.0, -1.0).astype(jnp.bfloat16)
    meta = [code] + bf16_parts(dense, 3)
    extra = 128
    filler = jnp.zeros((local_rows, extra - len(meta) * number), jnp.bfloat16)
    packed = jnp.concatenate([normed] + meta + [filler], axis=1)

    places = jnp.arange(capacity, dtype=jnp.float32)[:, None]

    def process(blocks):
        chosen, scales = [], []
        for block in blocks:
            info = lax.dynamic_slice_in_dim(block[:, width:], mine, number * len(meta), 1)
            cols = [info[:, j * number].astype(jnp.float32) for j in range(len(meta))]
            hit = cols[0][None, :] == places
            gate = (cols[1] + cols[2]) + cols[3]
            chosen.append(hit.astype(jnp.bfloat16))
            scales.append(jnp.sum(jnp.where(hit, gate[None, :], 0.0), axis=1))
        rows = [
            jnp.dot(ch, block[:, :width], preferred_element_type=jnp.float32)
            for ch, block in zip(chosen, blocks)
        ]
        rows = jnp.concatenate(rows, axis=0).astype(jnp.bfloat16)
        gated = jnp.dot(rows, w_gate[0], preferred_element_type=jnp.float32)
        upward = jnp.dot(rows, w_up[0], preferred_element_type=jnp.float32)
        hidden = (jax.nn.silu(gated) * upward).astype(jnp.bfloat16)
        out = jnp.dot(hidden, w_down[0], preferred_element_type=jnp.float32)
        out = (out * jnp.concatenate(scales)[:, None]).astype(jnp.bfloat16)
        result = []
        for i in range(len(blocks)):
            part_rows = out[i * capacity:(i + 1) * capacity]
            result.append(lax.dot_general(
                chosen[i], part_rows, (((0,), (0,)), ((), ())), preferred_element_type=jnp.float32
            ))
        return result

    other = send(packed, partner)
    pair_tok = jnp.stack([packed, other])
    contrib = {}
    half = ring // 2
    contrib[(0, 0)], contrib[(0, 1)] = process([packed, other])
    done = {0: [contrib[(0, 0)], contrib[(0, 1)]]}
    up_tok = pair_tok
    dn_tok = pair_tok
    arrived = {}
    for step in range(1, half):
        if step > 1:
            up_tok, dn_tok, _ = lax.optimization_barrier((up_tok, dn_tok, done[step - 2]))
        up_tok = send(up_tok, plus)
        dn_tok = send(dn_tok, minus)
        arrived[step] = [up_tok[0], up_tok[1], dn_tok[0], dn_tok[1]]
        if step < half - 2:
            done[step] = process(arrived[step])
    far = [send(up_tok[0], plus), send(dn_tok[1], minus)]
    ends = process(far[:1])
    far_other = lax.optimization_barrier((far[1], ends))[0]
    ends = ends + process([far_other])
    last_blocks = lax.optimization_barrier((arrived[half - 1], ends))[0]
    last = process(last_blocks)
    for step, result in [(s, done[s]) for s in range(1, half - 2)] + [(half - 1, last)]:
        (contrib[(-step, 0)], contrib[(-step, 1)],
         contrib[(step, 0)], contrib[(step, 1)]) = result
    contrib[(-half, 0)], contrib[(half, 1)] = ends

    dn_part = send(contrib[(-half, 0)].astype(jnp.bfloat16), minus)
    up_part = send(contrib[(half, 1)].astype(jnp.bfloat16), plus)
    late_blocks, dn_part, up_part = lax.optimization_barrier((arrived[half - 2], dn_part, up_part))
    step = half - 2
    (contrib[(-step, 0)], contrib[(-step, 1)],
     contrib[(step, 0)], contrib[(step, 1)]) = process(late_blocks)
    dn_acc = [dn_part.astype(jnp.float32) + contrib[(-(half - 1), 0)],
              contrib[(-(half - 1), 1)]]
    up_acc = [contrib[(half - 1, 0)],
              up_part.astype(jnp.float32) + contrib[(half - 1, 1)]]
    for step in range(half - 1, 1, -1):
        dn_part = send(jnp.stack(dn_acc).astype(jnp.bfloat16), minus)
        up_part = send(jnp.stack(up_acc).astype(jnp.bfloat16), plus)
        dn_acc = [dn_part[p].astype(jnp.float32) + contrib[(-(step - 1), p)] for p in range(2)]
        up_acc = [up_part[p].astype(jnp.float32) + contrib[(step - 1, p)] for p in range(2)]
    minus_cross = route(group, lambda i: ((i // 2 - 1) % ring) * 2 + 1 - i % 2)
    plus_cross = route(group, lambda i: ((i // 2 + 1) % ring) * 2 + 1 - i % 2)
    arriving = [
        send(dn_acc[0].astype(jnp.bfloat16), minus),
        send(up_acc[0].astype(jnp.bfloat16), plus),
        send(dn_acc[1].astype(jnp.bfloat16), minus_cross),
        send(up_acc[1].astype(jnp.bfloat16), plus_cross),
        send(contrib[(0, 1)].astype(jnp.bfloat16), partner),
    ]
    mixed = contrib[(0, 0)]
    for part in arriving:
        mixed = mixed + part.astype(jnp.float32)
    return mixed.astype(jnp.bfloat16)


def solution(mesh):
    return jax.shard_map(
        local,
        mesh=mesh,
        in_specs=(
            P(("dp", "expert"), None),
            P(),
            P(("dp", "expert"), None),
            P(("dp", "expert"), None),
            P("expert", None, None),
            P("expert", None, None),
            P("expert", None, None),
        ),
        out_specs=P(("dp", "expert"), None),
        check_vma=False,
    )
```

```python
import jax
import jax.numpy as jnp
from jax import lax
from jax.sharding import PartitionSpec as P

eps_value = 1e-06


def normalize(tokens, gain):
    values = tokens.astype(jnp.float32)
    meansq = jnp.mean(values * values, axis=-1, keepdims=True)
    return (values * lax.rsqrt(meansq + eps_value) * gain).astype(jnp.bfloat16)


def gate_dense(expert_ids, gate_values, number):
    labels = jnp.arange(number, dtype=jnp.int32)
    hits = (expert_ids[..., None] == labels).astype(jnp.float32)
    return jnp.sum(hits * gate_values[..., None], axis=-2)


def dispatch_table(column, capacity):
    matched = (column > 0).astype(jnp.float32)
    slots = jnp.cumsum(matched, axis=-1) - 1.0
    places = jnp.arange(capacity).astype(jnp.float32)
    chosen = (slots[..., None, :] == places[:, None]) & (matched[..., None, :] > 0)
    return chosen


def expert_mlp(slot_rows, gate_matrix, up_matrix, down_matrix):
    gated = jnp.dot(slot_rows, gate_matrix, preferred_element_type=jnp.float32)
    upward = jnp.dot(slot_rows, up_matrix, preferred_element_type=jnp.float32)
    hidden = (jax.nn.silu(gated) * upward).astype(jnp.bfloat16)
    return jnp.dot(hidden, down_matrix, preferred_element_type=jnp.float32).astype(jnp.bfloat16)


def bf16_parts(values, count):
    parts = []
    rest = values
    for _ in range(count):
        head = lax.reduce_precision(rest, exponent_bits=8, mantissa_bits=7)
        parts.append(head.astype(jnp.bfloat16))
        rest = rest - head
    return parts


def route(group, move):
    return [(i, move(i)) for i in range(group)]


def local(tokens, gain, expert_ids, gate_values, w_gate, w_up, w_down):
    group = lax.axis_size("expert")
    ring = group // 2
    position = lax.axis_index("expert")
    local_rows, width = tokens.shape
    chosen_count = expert_ids.shape[1]
    number = group * w_gate.shape[0]
    capacity = local_rows * chosen_count // number * 3 // 2
    mine = position

    partner = route(group, lambda i: i ^ 1)
    plus = route(group, lambda i: ((i // 2 + 1) % ring) * 2 + i % 2)
    minus = route(group, lambda i: ((i // 2 - 1) % ring) * 2 + i % 2)

    def send(x, perm):
        return lax.ppermute(x, "expert", perm)

    normed = normalize(tokens, gain)
    dense = gate_dense(expert_ids, gate_values, number)

    matched = dense > 0
    earlier = (jnp.arange(local_rows)[None, :] <= jnp.arange(local_rows)[:, None])
    rank = jnp.dot(earlier.astype(jnp.bfloat16), matched.astype(jnp.bfloat16),
                   preferred_element_type=jnp.float32)
    code = jnp.where(matched, rank - 1.0, -1.0).astype(jnp.bfloat16)
    meta = [code] + bf16_parts(dense, 3)
    extra = 128
    filler = jnp.zeros((local_rows, extra - len(meta) * number), jnp.bfloat16)
    packed = jnp.concatenate([normed] + meta + [filler], axis=1)

    places = jnp.arange(capacity, dtype=jnp.float32)[:, None]

    def process(blocks):
        chosen, scales = [], []
        for block in blocks:
            info = lax.dynamic_slice_in_dim(block[:, width:], mine, number * len(meta), 1)
            cols = [info[:, j * number].astype(jnp.float32) for j in range(len(meta))]
            hit = cols[0][None, :] == places
            gate = (cols[1] + cols[2]) + cols[3]
            chosen.append(hit.astype(jnp.bfloat16))
            scales.append(jnp.sum(jnp.where(hit, gate[None, :], 0.0), axis=1))
        rows = [
            jnp.dot(ch, block[:, :width], preferred_element_type=jnp.float32)
            for ch, block in zip(chosen, blocks)
        ]
        rows = jnp.concatenate(rows, axis=0).astype(jnp.bfloat16)
        gated = jnp.dot(rows, w_gate[0], preferred_element_type=jnp.float32)
        upward = jnp.dot(rows, w_up[0], preferred_element_type=jnp.float32)
        hidden = (jax.nn.silu(gated) * upward).astype(jnp.bfloat16)
        out = jnp.dot(hidden, w_down[0], preferred_element_type=jnp.float32)
        out = (out * jnp.concatenate(scales)[:, None]).astype(jnp.bfloat16)
        result = []
        for i in range(len(blocks)):
            part_rows = out[i * capacity:(i + 1) * capacity]
            result.append(lax.dot_general(
                chosen[i], part_rows, (((0,), (0,)), ((), ())), preferred_element_type=jnp.float32
            ))
        return result

    minus_cross = route(group, lambda i: ((i // 2 - 1) % ring) * 2 + 1 - i % 2)
    plus_cross = route(group, lambda i: ((i // 2 + 1) % ring) * 2 + 1 - i % 2)
    other = send(packed, partner)
    contrib = {}
    half = ring // 2
    contrib[(0, 0)], contrib[(0, 1)] = process([packed, other])
    done = {0: [contrib[(0, 0)], contrib[(0, 1)]]}
    up_tok = dn_tok = None
    arrived = {}
    for step in range(1, half):
        if step > 1:
            up_tok, dn_tok, _ = lax.optimization_barrier((up_tok, dn_tok, done[step - 2]))
        if step == 1:
            up_tok = jnp.stack([send(packed, plus), send(packed, plus_cross)])
            dn_tok = jnp.stack([send(packed, minus), send(packed, minus_cross)])
        else:
            up_tok = send(up_tok, plus)
            dn_tok = send(dn_tok, minus)
        arrived[step] = [up_tok[0], up_tok[1], dn_tok[0], dn_tok[1]]
        if step < half - 2:
            done[step] = process(arrived[step])
    far = [send(up_tok[0], plus), send(dn_tok[1], minus)]
    ends = process(far[:1])
    far_other = lax.optimization_barrier((far[1], ends))[0]
    ends = ends + process([far_other])
    last_blocks = lax.optimization_barrier((arrived[half - 1], ends))[0]
    last = process(last_blocks)
    for step, result in [(s, done[s]) for s in range(1, half - 2)] + [(half - 1, last)]:
        (contrib[(-step, 0)], contrib[(-step, 1)],
         contrib[(step, 0)], contrib[(step, 1)]) = result
    contrib[(-half, 0)], contrib[(half, 1)] = ends

    dn_part = send(contrib[(-half, 0)].astype(jnp.bfloat16), minus)
    up_part = send(contrib[(half, 1)].astype(jnp.bfloat16), plus)
    late_blocks, dn_part, up_part = lax.optimization_barrier((arrived[half - 2], dn_part, up_part))
    step = half - 2
    (contrib[(-step, 0)], contrib[(-step, 1)],
     contrib[(step, 0)], contrib[(step, 1)]) = process(late_blocks)
    dn_acc = [dn_part.astype(jnp.float32) + contrib[(-(half - 1), 0)],
              contrib[(-(half - 1), 1)]]
    up_acc = [contrib[(half - 1, 0)],
              up_part.astype(jnp.float32) + contrib[(half - 1, 1)]]
    for step in range(half - 1, 1, -1):
        dn_part = send(jnp.stack(dn_acc).astype(jnp.bfloat16), minus)
        up_part = send(jnp.stack(up_acc).astype(jnp.bfloat16), plus)
        dn_acc = [dn_part[p].astype(jnp.float32) + contrib[(-(step - 1), p)] for p in range(2)]
        up_acc = [up_part[p].astype(jnp.float32) + contrib[(step - 1, p)] for p in range(2)]
    arriving = [
        send(dn_acc[0].astype(jnp.bfloat16), minus),
        send(up_acc[0].astype(jnp.bfloat16), plus),
        send(dn_acc[1].astype(jnp.bfloat16), minus_cross),
        send(up_acc[1].astype(jnp.bfloat16), plus_cross),
        send(contrib[(0, 1)].astype(jnp.bfloat16), partner),
    ]
    mixed = contrib[(0, 0)]
    for part in arriving:
        mixed = mixed + part.astype(jnp.float32)
    return mixed.astype(jnp.bfloat16)


def solution(mesh):
    return jax.shard_map(
        local,
        mesh=mesh,
        in_specs=(
            P(("dp", "expert"), None),
            P(),
            P(("dp", "expert"), None),
            P(("dp", "expert"), None),
            P("expert", None, None),
            P("expert", None, None),
            P("expert", None, None),
        ),
        out_specs=P(("dp", "expert"), None),
        check_vma=False,
    )
```

```python
import jax
import jax.numpy as jnp
from jax import lax
from jax.sharding import PartitionSpec as P

eps_value = 1e-06


def normalize(tokens, gain):
    values = tokens.astype(jnp.float32)
    meansq = jnp.mean(values * values, axis=-1, keepdims=True)
    return (values * lax.rsqrt(meansq + eps_value) * gain).astype(jnp.bfloat16)


def gate_dense(expert_ids, gate_values, number):
    labels = jnp.arange(number, dtype=jnp.int32)
    hits = (expert_ids[..., None] == labels).astype(jnp.float32)
    return jnp.sum(hits * gate_values[..., None], axis=-2)


def dispatch_table(column, capacity):
    matched = (column > 0).astype(jnp.float32)
    slots = jnp.cumsum(matched, axis=-1) - 1.0
    places = jnp.arange(capacity).astype(jnp.float32)
    chosen = (slots[..., None, :] == places[:, None]) & (matched[..., None, :] > 0)
    return chosen


def expert_mlp(slot_rows, gate_matrix, up_matrix, down_matrix):
    gated = jnp.dot(slot_rows, gate_matrix, preferred_element_type=jnp.float32)
    upward = jnp.dot(slot_rows, up_matrix, preferred_element_type=jnp.float32)
    hidden = (jax.nn.silu(gated) * upward).astype(jnp.bfloat16)
    return jnp.dot(hidden, down_matrix, preferred_element_type=jnp.float32).astype(jnp.bfloat16)


def bf16_parts(values, count):
    parts = []
    rest = values
    for _ in range(count):
        head = lax.reduce_precision(rest, exponent_bits=8, mantissa_bits=7)
        parts.append(head.astype(jnp.bfloat16))
        rest = rest - head
    return parts


def route(group, move):
    return [(i, move(i)) for i in range(group)]


def local(tokens, gain, expert_ids, gate_values, w_gate, w_up, w_down):
    group = lax.axis_size("expert")
    ring = group // 2
    position = lax.axis_index("expert")
    local_rows, width = tokens.shape
    chosen_count = expert_ids.shape[1]
    number = group * w_gate.shape[0]
    capacity = local_rows * chosen_count // number * 3 // 2
    mine = position

    partner = route(group, lambda i: i ^ 1)
    plus = route(group, lambda i: ((i // 2 + 1) % ring) * 2 + i % 2)
    minus = route(group, lambda i: ((i // 2 - 1) % ring) * 2 + i % 2)

    def send(x, perm):
        return lax.ppermute(x, "expert", perm)

    normed = normalize(tokens, gain)
    dense = gate_dense(expert_ids, gate_values, number)

    matched = dense > 0
    earlier = (jnp.arange(local_rows)[None, :] <= jnp.arange(local_rows)[:, None])
    rank = jnp.dot(earlier.astype(jnp.bfloat16), matched.astype(jnp.bfloat16),
                   preferred_element_type=jnp.float32)
    code = jnp.where(matched, rank - 1.0, -1.0).astype(jnp.bfloat16)
    meta = [code] + bf16_parts(dense, 3)
    extra = 128
    filler = jnp.zeros((local_rows, extra - len(meta) * number), jnp.bfloat16)
    packed = jnp.concatenate([normed] + meta + [filler], axis=1)

    places = jnp.arange(capacity, dtype=jnp.float32)[:, None]

    def process(blocks):
        chosen, scales = [], []
        for block in blocks:
            info = lax.dynamic_slice_in_dim(block[:, width:], mine, number * len(meta), 1)
            cols = [info[:, j * number].astype(jnp.float32) for j in range(len(meta))]
            hit = cols[0][None, :] == places
            gate = (cols[1] + cols[2]) + cols[3]
            chosen.append(hit.astype(jnp.bfloat16))
            scales.append(jnp.sum(jnp.where(hit, gate[None, :], 0.0), axis=1))
        rows = [
            jnp.dot(ch, block[:, :width], preferred_element_type=jnp.float32)
            for ch, block in zip(chosen, blocks)
        ]
        rows = jnp.concatenate(rows, axis=0).astype(jnp.bfloat16)
        gated = jnp.dot(rows, w_gate[0], preferred_element_type=jnp.float32)
        upward = jnp.dot(rows, w_up[0], preferred_element_type=jnp.float32)
        hidden = (jax.nn.silu(gated) * upward).astype(jnp.bfloat16)
        out = jnp.dot(hidden, w_down[0], preferred_element_type=jnp.float32)
        out = (out * jnp.concatenate(scales)[:, None]).astype(jnp.bfloat16)
        result = []
        for i in range(len(blocks)):
            part_rows = out[i * capacity:(i + 1) * capacity]
            result.append(lax.dot_general(
                chosen[i], part_rows, (((0,), (0,)), ((), ())), preferred_element_type=jnp.float32
            ))
        return result

    other = send(packed, partner)
    pair_tok = jnp.stack([packed, other])
    contrib = {}
    half = ring // 2
    contrib[(0, 0)], contrib[(0, 1)] = process([packed, other])
    done = {0: [contrib[(0, 0)], contrib[(0, 1)]]}
    up_tok = pair_tok
    dn_tok = pair_tok
    arrived = {}
    for step in range(1, half):
        if step > 1:
            up_tok, dn_tok, _ = lax.optimization_barrier((up_tok, dn_tok, done[step - 2]))
        up_tok = send(up_tok, plus)
        dn_tok = send(dn_tok, minus)
        arrived[step] = [up_tok[0], up_tok[1], dn_tok[0], dn_tok[1]]
        if step < half - 2:
            done[step] = process(arrived[step])
    far = [send(up_tok[0], plus), send(dn_tok[1], minus)]
    ends = process(far)
    last_blocks = lax.optimization_barrier((arrived[half - 1], ends))[0]
    last = process(last_blocks)
    for step, result in [(s, done[s]) for s in range(1, half - 2)] + [(half - 1, last)]:
        (contrib[(-step, 0)], contrib[(-step, 1)],
         contrib[(step, 0)], contrib[(step, 1)]) = result
    contrib[(-half, 0)], contrib[(half, 1)] = ends

    dn_part = send(contrib[(-half, 0)].astype(jnp.bfloat16), minus)
    up_part = send(contrib[(half, 1)].astype(jnp.bfloat16), plus)
    late_blocks, dn_part, up_part = lax.optimization_barrier((arrived[half - 2], dn_part, up_part))
    step = half - 2
    (contrib[(-step, 0)], contrib[(-step, 1)],
     contrib[(step, 0)], contrib[(step, 1)]) = process(late_blocks)
    dn_acc = [dn_part.astype(jnp.float32) + contrib[(-(half - 1), 0)],
              contrib[(-(half - 1), 1)]]
    up_acc = [contrib[(half - 1, 0)],
              up_part.astype(jnp.float32) + contrib[(half - 1, 1)]]
    for step in range(half - 1, 1, -1):
        dn_part = send(jnp.stack(dn_acc).astype(jnp.bfloat16), minus)
        up_part = send(jnp.stack(up_acc).astype(jnp.bfloat16), plus)
        dn_acc = [dn_part[p].astype(jnp.float32) + contrib[(-(step - 1), p)] for p in range(2)]
        up_acc = [up_part[p].astype(jnp.float32) + contrib[(step - 1, p)] for p in range(2)]
    minus_cross = route(group, lambda i: ((i // 2 - 1) % ring) * 2 + 1 - i % 2)
    plus_cross = route(group, lambda i: ((i // 2 + 1) % ring) * 2 + 1 - i % 2)
    arriving = [
        send(dn_acc[0].astype(jnp.bfloat16), minus),
        send(up_acc[0].astype(jnp.bfloat16), plus),
        send(dn_acc[1].astype(jnp.bfloat16), minus_cross),
        send(up_acc[1].astype(jnp.bfloat16), plus_cross),
        send(contrib[(0, 1)].astype(jnp.bfloat16), partner),
    ]
    mixed = contrib[(0, 0)]
    for part in arriving:
        mixed = mixed + part.astype(jnp.float32)
    return mixed.astype(jnp.bfloat16)


def solution(mesh):
    return jax.shard_map(
        local,
        mesh=mesh,
        in_specs=(
            P(("dp", "expert"), None),
            P(),
            P(("dp", "expert"), None),
            P(("dp", "expert"), None),
            P("expert", None, None),
            P("expert", None, None),
            P("expert", None, None),
        ),
        out_specs=P(("dp", "expert"), None),
        check_vma=False,
    )
```
